128 devices in a mesh: row: 8 (over x_lo, z), col: 16 (over y, x_hi, core).
Axes of the slice: x: 4 (x_hi: 2, x_lo: 2; x = x_hi * 2 + x_lo), y: 4, z: 4, core: 2. Of those that a mesh axis runs over, the one named last changes fastest.
Arguments:
- adjusted_rows: bfloat16 [8192, 29568], P(('row', 'col')), may hold values from -5 to 5
- base_weight: bfloat16 [8192, 29568], P('row', 'col'), may hold values from -5 to 5
- range_test: bfloat16 [29568, 384], P('col'), may hold values from -0.03125 to 0.03125
- corange_test: bfloat16 [384, 8192], P(None, 'row'), may hold values from -0.0625 to 0.0625
- core_left: bfloat16 [768, 8192], P(None, 'row'), may hold values from -0.0625 to 0.0625
- core_right: bfloat16 [768, 29568], P(None, 'col'), may hold values from -1 to 1
Outputs:
- range_sketch: float32 [8192, 384], P('row')
- corange_sketch: float32 [384, 29568], P(None, 'col')
- core_solution: float32 [384, 768], P(None, 'col')
The draws below stay inside these ranges and needn't reach their ends.
All inputs are finite; a program needn't handle non-finite values.
Results may differ from the reference program's by a relative error of at most 0.0066.
Values may be sent and summed in bfloat16 or wider, within the bound.
No kernel may reach another device: no remote copies, remote signals or barrier semaphores. Data moves between devices by JAX's collectives and lax.ppermute only.
A program may use at most 128 MiB of HBM per device.

```python
import jax
import jax.numpy as jnp
from jax import lax

R = 8192
C = 29568
K = 384
S = 768


def steps_of(rng, shape, split, smallest, top_value):
    factor_of, own = 1.0, jax.random.fold_in(rng, 6)
    for axis_at, parts in split:
        heights = jnp.exp(jax.random.uniform(jax.random.fold_in(own, axis_at), (parts,), jnp.float32, smallest / len(split), top_value / len(split)))
        factor_of = factor_of * jnp.repeat(heights, shape[axis_at] // parts).reshape([-1 if axis == axis_at else 1 for axis in range(len(shape))])
    return factor_of


def bell_draw(key, shape, width, bound, shards=(), dtype=jnp.bfloat16):
    level = steps_of(key, shape, shards, -0.22, 0.18) if shards else 1.0
    values = jax.random.normal(key, shape, jnp.float32) * width * level
    return jnp.minimum(jnp.maximum(values, -bound), bound).astype(dtype)


def setup_inputs(seed: int = 0) -> dict:
    key_of = jax.random.split(jax.random.key(seed), 7)
    adjusted_rows = bell_draw(key_of[0], (R, C), 0.7, 5.0, ((0, 128),))
    base_weight = bell_draw(key_of[1], (R, C), 0.7, 5.0, ((0, 8), (1, 16)))
    range_test = bell_draw(key_of[2], (C, K), C ** -0.5, 0.03125, ((0, 16),))
    corange_test = bell_draw(key_of[3], (K, R), R ** -0.5, 0.0625, ((1, 8),))
    core_left = bell_draw(key_of[4], (S, R), R ** -0.5, 0.0625, ((1, 8),))
    core_right = bell_draw(key_of[5], (S, C), (C // S) ** -0.5, 1.0, ((1, 16),))
    return dict(adjusted_rows=adjusted_rows, base_weight=base_weight, range_test=range_test, corange_test=corange_test, core_left=core_left, core_right=core_right)


def reference(adjusted_rows, base_weight, range_test, corange_test, core_left, core_right):
    highest = lax.Precision.HIGHEST
    difference = (adjusted_rows.astype(jnp.float32) - base_weight.astype(jnp.float32)).astype(jnp.bfloat16)
    range_sketch = jnp.dot(difference.astype(jnp.float32), range_test.astype(jnp.float32), preferred_element_type=jnp.float32)
    corange_sketch = jnp.dot(corange_test.astype(jnp.float32), difference.astype(jnp.float32), preferred_element_type=jnp.float32)
    left_product = jnp.dot(core_left.astype(jnp.float32), difference.astype(jnp.float32), preferred_element_type=jnp.float32)
    core_sketch = jnp.dot(left_product, core_right.astype(jnp.float32).T, precision=highest)
    projected = jnp.dot(core_left.astype(jnp.float32), range_sketch, precision=highest)
    gram_matrix = jnp.dot(projected.T, projected, precision=highest)
    right_hand = jnp.dot(projected.T, core_sketch, precision=highest)
    factor = jnp.linalg.cholesky(gram_matrix)
    halfway = lax.linalg.triangular_solve(factor, right_hand, left_side=True, lower=True)
    core_solution = lax.linalg.triangular_solve(factor, halfway, left_side=True, lower=True, transpose_a=True)
    return (range_sketch, corange_sketch, core_solution)
```

```python
import jax
import jax.numpy as jnp
from jax import lax
from jax.sharding import PartitionSpec as P

S = 768


def scatter_sum(part, axis, groups):
    rows = part.shape[0] // groups
    got = lax.all_to_all(part, axis, split_axis=0, concat_axis=0, tiled=True)
    return got.reshape(groups, rows, *part.shape[1:]).sum(axis=0)


def gather_rows(chunk, axis, groups):
    tiled = jnp.broadcast_to(chunk[None], (groups, *chunk.shape)).reshape(
        groups * chunk.shape[0], *chunk.shape[1:]
    )
    return lax.all_to_all(tiled, axis, split_axis=0, concat_axis=0, tiled=True)


def local(adjusted_rows, base_weight, range_test, corange_test, core_left, core_right):
    highest = lax.Precision.HIGHEST
    ncol = lax.axis_size("col")
    nrow = lax.axis_size("row")
    adjusted_block = lax.all_to_all(adjusted_rows, "col", split_axis=1, concat_axis=0, tiled=True)
    difference = (adjusted_block.astype(jnp.float32) - base_weight.astype(jnp.float32)).astype(
        jnp.bfloat16
    )
    range_part = jnp.dot(difference, range_test, preferred_element_type=jnp.float32)
    range_chunk = scatter_sum(range_part, "col", ncol)
    range_sketch = gather_rows(range_chunk, "col", ncol)
    corange_part = jnp.dot(corange_test, difference, preferred_element_type=jnp.float32)
    corange_sketch = lax.psum(corange_part, "row")
    left_float = core_left.astype(jnp.float32)
    projected_part = jnp.dot(left_float, range_sketch, precision=highest)
    projected = gather_rows(scatter_sum(projected_part, "row", nrow), "row", nrow)
    left_product = jnp.dot(core_left, difference, preferred_element_type=jnp.float32)
    partial_value = jnp.dot(left_product, core_right.astype(jnp.float32).T, precision=highest)
    own_columns = lax.psum_scatter(partial_value, "col", scatter_dimension=1, tiled=True)
    own_columns = lax.psum(own_columns, "row")
    gram_matrix = jnp.dot(projected.T, projected, precision=highest)
    right_hand = jnp.dot(projected.T, own_columns, precision=highest)
    factor = jnp.linalg.cholesky(gram_matrix)
    halfway = lax.linalg.triangular_solve(factor, right_hand, left_side=True, lower=True)
    core_solution = lax.linalg.triangular_solve(
        factor, halfway, left_side=True, lower=True, transpose_a=True
    )
    return (range_sketch, corange_sketch, core_solution)


def solution(mesh):
    in_specs = (
        P(("row", "col"), None),
        P("row", "col"),
        P("col", None),
        P(None, "row"),
        P(None, "row"),
        P(None, "col"),
    )
    out_specs = (P("row", None), P(None, "col"), P(None, "col"))
    return jax.shard_map(local, mesh=mesh, in_specs=in_specs, out_specs=out_specs, check_vma=False)
```

```python
import jax
import jax.numpy as jnp
from jax import lax
from jax.sharding import PartitionSpec as P

S = 768


def scatter_sum(part, axis, groups):
    rows = part.shape[0] // groups
    got = lax.all_to_all(part, axis, split_axis=0, concat_axis=0, tiled=True)
    return got.reshape(groups, rows, *part.shape[1:]).sum(axis=0)


def gather_rows(chunk, axis, groups):
    tiled = jnp.broadcast_to(chunk[None], (groups, *chunk.shape)).reshape(
        groups * chunk.shape[0], *chunk.shape[1:]
    )
    return lax.all_to_all(tiled, axis, split_axis=0, concat_axis=0, tiled=True)


def local(adjusted_rows, base_weight, range_test, corange_test, core_left, core_right):
    highest = lax.Precision.HIGHEST
    ncol = lax.axis_size("col")
    nrow = lax.axis_size("row")
    height, width = adjusted_rows.shape[0], adjusted_rows.shape[1] // ncol
    by_target = adjusted_rows.reshape(height, ncol, width).transpose(1, 0, 2)
    adjusted_block = lax.all_to_all(by_target, "col", split_axis=0, concat_axis=0, tiled=True)
    adjusted_block = adjusted_block.reshape(ncol * height, width)
    difference = (adjusted_block.astype(jnp.float32) - base_weight.astype(jnp.float32)).astype(
        jnp.bfloat16
    )
    range_part = jnp.dot(difference, range_test, preferred_element_type=jnp.float32)
    range_chunk = scatter_sum(range_part, "col", ncol)
    range_sketch = gather_rows(range_chunk, "col", ncol)
    corange_part = jnp.dot(corange_test, difference, preferred_element_type=jnp.float32)
    corange_sketch = lax.psum(corange_part, "row")
    left_float = core_left.astype(jnp.float32)
    projected_part = jnp.dot(left_float, range_part, precision=highest)
    every = ("row", "col")
    projected = gather_rows(scatter_sum(projected_part, every, nrow * ncol), every, nrow * ncol)
    left_product = jnp.dot(core_left, difference, preferred_element_type=jnp.float32)
    partial_value = jnp.dot(left_product, core_right.astype(jnp.float32).T, precision=highest)
    own_columns = lax.psum_scatter(partial_value, "col", scatter_dimension=1, tiled=True)
    own_columns = gather_rows(scatter_sum(own_columns, "row", nrow), "row", nrow)
    gram_matrix = jnp.dot(projected.T, projected, precision=highest)
    right_hand = jnp.dot(projected.T, own_columns, precision=highest)
    factor = jnp.linalg.cholesky(gram_matrix)
    halfway = lax.linalg.triangular_solve(factor, right_hand, left_side=True, lower=True)
    core_solution = lax.linalg.triangular_solve(
        factor, halfway, left_side=True, lower=True, transpose_a=True
    )
    return (range_sketch, corange_sketch, core_solution)


def solution(mesh):
    in_specs = (
        P(("row", "col"), None),
        P("row", "col"),
        P("col", None),
        P(None, "row"),
        P(None, "row"),
        P(None, "col"),
    )
    out_specs = (P("row", None), P(None, "col"), P(None, "col"))
    return jax.shard_map(local, mesh=mesh, in_specs=in_specs, out_specs=out_specs, check_vma=False)
```

```python
import jax
import jax.numpy as jnp
from jax import lax
from jax.sharding import PartitionSpec as P

S = 768


def scatter_sum(part, axis, groups):
    rows = part.shape[0] // groups
    got = lax.all_to_all(part, axis, split_axis=0, concat_axis=0, tiled=True)
    return got.reshape(groups, rows, *part.shape[1:]).sum(axis=0)


def gather_rows(chunk, axis, groups):
    tiled = jnp.broadcast_to(chunk[None], (groups, *chunk.shape)).reshape(
        groups * chunk.shape[0], *chunk.shape[1:]
    )
    return lax.all_to_all(tiled, axis, split_axis=0, concat_axis=0, tiled=True)


def local(adjusted_rows, base_weight, range_test, corange_test, core_left, core_right):
    highest = lax.Precision.HIGHEST
    ncol = lax.axis_size("col")
    nrow = lax.axis_size("row")
    height, width = adjusted_rows.shape[0], adjusted_rows.shape[1] // ncol
    by_target = adjusted_rows.reshape(height, ncol, width).transpose(1, 0, 2)
    adjusted_block = lax.all_to_all(by_target, "col", split_axis=0, concat_axis=0, tiled=True)
    adjusted_block = adjusted_block.reshape(ncol * height, width)
    difference = (adjusted_block.astype(jnp.float32) - base_weight.astype(jnp.float32)).astype(
        jnp.bfloat16
    )
    range_part = jnp.dot(difference, range_test, preferred_element_type=jnp.float32)
    corange_part = jnp.dot(corange_test, difference, preferred_element_type=jnp.float32)
    left_float = core_left.astype(jnp.float32)
    projected_part = jnp.dot(left_float, range_part, precision=highest)
    every = ("row", "col")
    projected = gather_rows(scatter_sum(projected_part, every, nrow * ncol), every, nrow * ncol)
    left_product = jnp.dot(core_left, difference, preferred_element_type=jnp.float32)
    partial_value = jnp.dot(left_product, core_right.astype(jnp.float32).T, precision=highest)
    own_columns = lax.psum_scatter(partial_value, "col", scatter_dimension=1, tiled=True)
    projected, range_part, corange_part = lax.optimization_barrier(
        (projected, range_part, corange_part)
    )
    range_sketch = gather_rows(scatter_sum(range_part, "col", ncol), "col", ncol)
    corange_sketch = gather_rows(scatter_sum(corange_part, "row", nrow), "row", nrow)
    own_columns = gather_rows(scatter_sum(own_columns, "row", nrow), "row", nrow)
    gram_matrix = jnp.dot(projected.T, projected, precision=highest)
    right_hand = jnp.dot(projected.T, own_columns, precision=highest)
    factor = jnp.linalg.cholesky(gram_matrix)
    halfway = lax.linalg.triangular_solve(factor, right_hand, left_side=True, lower=True)
    core_solution = lax.linalg.triangular_solve(
        factor, halfway, left_side=True, lower=True, transpose_a=True
    )
    return (range_sketch, corange_sketch, core_solution)


def solution(mesh):
    in_specs = (
        P(("row", "col"), None),
        P("row", "col"),
        P("col", None),
        P(None, "row"),
        P(None, "row"),
        P(None, "col"),
    )
    out_specs = (P("row", None), P(None, "col"), P(None, "col"))
    return jax.shard_map(local, mesh=mesh, in_specs=in_specs, out_specs=out_specs, check_vma=False)
```

```python
import jax
import jax.numpy as jnp
from jax import lax
from jax.sharding import PartitionSpec as P

S = 768


def scatter_sum(part, axis, groups):
    rows = part.shape[0] // groups
    got = lax.all_to_all(part, axis, split_axis=0, concat_axis=0, tiled=True)
    return got.reshape(groups, rows, *part.shape[1:]).sum(axis=0)


def gather_rows(chunk, axis, groups):
    tiled = jnp.broadcast_to(chunk[None], (groups, *chunk.shape)).reshape(
        groups * chunk.shape[0], *chunk.shape[1:]
    )
    return lax.all_to_all(tiled, axis, split_axis=0, concat_axis=0, tiled=True)


def local(adjusted_rows, base_weight, range_test, corange_test, core_left, core_right):
    highest = lax.Precision.HIGHEST
    ncol = lax.axis_size("col")
    nrow = lax.axis_size("row")
    height, width = adjusted_rows.shape[0], adjusted_rows.shape[1] // ncol
    by_target = adjusted_rows.reshape(height, ncol, width).transpose(1, 0, 2)
    adjusted_block = lax.all_to_all(by_target, "col", split_axis=0, concat_axis=0, tiled=True)
    adjusted_block = adjusted_block.reshape(ncol * height, width)
    difference = (adjusted_block.astype(jnp.float32) - base_weight.astype(jnp.float32)).astype(
        jnp.bfloat16
    )
    range_part = jnp.dot(difference, range_test, preferred_element_type=jnp.float32)
    corange_part = jnp.dot(corange_test, difference, preferred_element_type=jnp.float32)
    left_float = core_left.astype(jnp.float32)
    projected_part = jnp.dot(left_float, range_part, precision=highest)
    every = ("row", "col")
    projected = gather_rows(scatter_sum(projected_part, every, nrow * ncol), every, nrow * ncol)
    left_product = jnp.dot(core_left, difference, preferred_element_type=jnp.float32)
    partial_value = jnp.dot(left_product, core_right.astype(jnp.float32).T, precision=highest)
    corange_sketch = lax.psum(corange_part, "row")
    projected, range_part, partial_value = lax.optimization_barrier(
        (projected, range_part, partial_value)
    )
    cols = partial_value.shape[1] // ncol
    by_owner = partial_value.reshape(S, ncol, cols).transpose(1, 0, 2).reshape(ncol * S, cols)
    own_columns = scatter_sum(by_owner, "col", ncol)
    own_columns = gather_rows(scatter_sum(own_columns, "row", nrow), "row", nrow)
    range_sketch = gather_rows(scatter_sum(range_part, "col", ncol), "col", ncol)
    gram_matrix = jnp.dot(projected.T, projected, precision=highest)
    right_hand = jnp.dot(projected.T, own_columns, precision=highest)
    factor = jnp.linalg.cholesky(gram_matrix)
    halfway = lax.linalg.triangular_solve(factor, right_hand, left_side=True, lower=True)
    core_solution = lax.linalg.triangular_solve(
        factor, halfway, left_side=True, lower=True, transpose_a=True
    )
    return (range_sketch, corange_sketch, core_solution)


def solution(mesh):
    in_specs = (
        P(("row", "col"), None),
        P("row", "col"),
        P("col", None),
        P(None, "row"),
        P(None, "row"),
        P(None, "col"),
    )
    out_specs = (P("row", None), P(None, "col"), P(None, "col"))
    return jax.shard_map(local, mesh=mesh, in_specs=in_specs, out_specs=out_specs, check_vma=False)
```

```python
import jax
import jax.numpy as jnp
from jax import lax
from jax.sharding import PartitionSpec as P

S = 768


def scatter_sum(part, axis, groups):
    rows = part.shape[0] // groups
    got = lax.all_to_all(part, axis, split_axis=0, concat_axis=0, tiled=True)
    return got.reshape(groups, rows, *part.shape[1:]).sum(axis=0)


def gather_rows(chunk, axis, groups):
    tiled = jnp.broadcast_to(chunk[None], (groups, *chunk.shape)).reshape(
        groups * chunk.shape[0], *chunk.shape[1:]
    )
    return lax.all_to_all(tiled, axis, split_axis=0, concat_axis=0, tiled=True)


def dot_hi(a, b):
    return jnp.dot(a, b, precision=lax.Precision.HIGHEST)


def cholesky_solve(gram, rhs, size=128):
    count = gram.shape[0] // size
    gram = (gram + gram.T) * 0.5
    block = lambda i, j: gram[i * size:(i + 1) * size, j * size:(j + 1) * size]
    eye = jnp.eye(size, dtype=gram.dtype)
    low = {}
    inverse = []
    for j in range(count):
        a = block(j, j)
        for m in range(j):
            a = a - dot_hi(low[j, m], low[j, m].T)
        low[j, j] = lax.linalg.cholesky(a, symmetrize_input=False)
        inverse.append(lax.linalg.triangular_solve(low[j, j], eye, left_side=True, lower=True))
        for i in range(j + 1, count):
            a = block(i, j)
            for m in range(j):
                a = a - dot_hi(low[i, m], low[j, m].T)
            low[i, j] = dot_hi(a, inverse[j].T)
    halfway = []
    for i in range(count):
        r = rhs[i * size:(i + 1) * size]
        for m in range(i):
            r = r - dot_hi(low[i, m], halfway[m])
        halfway.append(dot_hi(inverse[i], r))
    result = [None] * count
    for i in reversed(range(count)):
        r = halfway[i]
        for m in range(i + 1, count):
            r = r - dot_hi(low[m, i].T, result[m])
        result[i] = dot_hi(inverse[i].T, r)
    return jnp.concatenate(result, axis=0)


def local(adjusted_rows, base_weight, range_test, corange_test, core_left, core_right):
    highest = lax.Precision.HIGHEST
    ncol = lax.axis_size("col")
    nrow = lax.axis_size("row")
    height, width = adjusted_rows.shape[0], adjusted_rows.shape[1] // ncol
    by_target = adjusted_rows.reshape(height, ncol, width).transpose(1, 0, 2)
    adjusted_block = lax.all_to_all(by_target, "col", split_axis=0, concat_axis=0, tiled=True)
    adjusted_block = adjusted_block.reshape(ncol * height, width)
    difference = (adjusted_block.astype(jnp.float32) - base_weight.astype(jnp.float32)).astype(
        jnp.bfloat16
    )
    range_part = jnp.dot(difference, range_test, preferred_element_type=jnp.float32)
    corange_part = jnp.dot(corange_test, difference, preferred_element_type=jnp.float32)
    left_float = core_left.astype(jnp.float32)
    projected_part = jnp.dot(left_float, range_part, precision=highest)
    every = ("row", "col")
    projected = gather_rows(scatter_sum(projected_part, every, nrow * ncol), every, nrow * ncol)
    left_product = jnp.dot(core_left, difference, preferred_element_type=jnp.float32)
    partial_value = jnp.dot(left_product, core_right.astype(jnp.float32).T, precision=highest)
    corange_sketch = lax.psum(corange_part, "row")
    projected, range_part, partial_value = lax.optimization_barrier(
        (projected, range_part, partial_value)
    )
    cols = partial_value.shape[1] // ncol
    by_owner = partial_value.reshape(S, ncol, cols).transpose(1, 0, 2).reshape(ncol * S, cols)
    own_columns = scatter_sum(by_owner, "col", ncol)
    own_columns = gather_rows(scatter_sum(own_columns, "row", nrow), "row", nrow)
    range_sketch = gather_rows(scatter_sum(range_part, "col", ncol), "col", ncol)
    gram_matrix = jnp.dot(projected.T, projected, precision=highest)
    right_hand = jnp.dot(projected.T, own_columns, precision=highest)
    core_solution = cholesky_solve(gram_matrix, right_hand)
    return (range_sketch, corange_sketch, core_solution)


def solution(mesh):
    in_specs = (
        P(("row", "col"), None),
        P("row", "col"),
        P("col", None),
        P(None, "row"),
        P(None, "row"),
        P(None, "col"),
    )
    out_specs = (P("row", None), P(None, "col"), P(None, "col"))
    return jax.shard_map(local, mesh=mesh, in_specs=in_specs, out_specs=out_specs, check_vma=False)
```

```python
import jax
import jax.numpy as jnp
from jax import lax
from jax.sharding import PartitionSpec as P

S = 768


def scatter_sum(part, axis, groups):
    rows = part.shape[0] // groups
    got = lax.all_to_all(part, axis, split_axis=0, concat_axis=0, tiled=True)
    return got.reshape(groups, rows, *part.shape[1:]).sum(axis=0)


def gather_rows(chunk, axis, groups):
    tiled = jnp.broadcast_to(chunk[None], (groups, *chunk.shape)).reshape(
        groups * chunk.shape[0], *chunk.shape[1:]
    )
    return lax.all_to_all(tiled, axis, split_axis=0, concat_axis=0, tiled=True)


def dot_hi(a, b):
    return jnp.dot(a, b, precision=lax.Precision.HIGHEST)


def cholesky_solve(gram, rhs, size=128):
    count = gram.shape[0] // size
    gram = (gram + gram.T) * 0.5
    block = lambda i, j: gram[i * size:(i + 1) * size, j * size:(j + 1) * size]
    eye = jnp.eye(size, dtype=gram.dtype)
    low = {}
    inverse = []
    for j in range(count):
        a = block(j, j)
        for m in range(j):
            a = a - dot_hi(low[j, m], low[j, m].T)
        low[j, j] = lax.linalg.cholesky(a, symmetrize_input=False)
        inverse.append(lax.linalg.triangular_solve(low[j, j], eye, left_side=True, lower=True))
        for i in range(j + 1, count):
            a = block(i, j)
            for m in range(j):
                a = a - dot_hi(low[i, m], low[j, m].T)
            low[i, j] = dot_hi(a, inverse[j].T)
    halfway = []
    for i in range(count):
        r = rhs[i * size:(i + 1) * size]
        for m in range(i):
            r = r - dot_hi(low[i, m], halfway[m])
        halfway.append(dot_hi(inverse[i], r))
    result = [None] * count
    for i in reversed(range(count)):
        r = halfway[i]
        for m in range(i + 1, count):
            r = r - dot_hi(low[m, i].T, result[m])
        result[i] = dot_hi(inverse[i].T, r)
    return jnp.concatenate(result, axis=0)


def local(adjusted_rows, base_weight, range_test, corange_test, core_left, core_right):
    highest = lax.Precision.HIGHEST
    ncol = lax.axis_size("col")
    nrow = lax.axis_size("row")
    height, width = adjusted_rows.shape[0], adjusted_rows.shape[1] // ncol
    by_target = adjusted_rows.reshape(height, ncol, width).transpose(1, 0, 2)
    adjusted_block = lax.all_to_all(by_target, "col", split_axis=0, concat_axis=0, tiled=True)
    adjusted_block = adjusted_block.reshape(ncol * height, width)
    difference = (adjusted_block.astype(jnp.float32) - base_weight.astype(jnp.float32)).astype(
        jnp.bfloat16
    )
    left_product = jnp.dot(core_left, difference, preferred_element_type=jnp.float32)
    partial_value = jnp.dot(left_product, core_right.astype(jnp.float32).T, precision=highest)
    own_columns = lax.psum_scatter(partial_value, "col", scatter_dimension=1, tiled=True)
    corange_part = jnp.dot(corange_test, difference, preferred_element_type=jnp.float32)
    corange_sketch = lax.psum(corange_part, "row")
    range_part = jnp.dot(difference, range_test, preferred_element_type=jnp.float32)
    left_float = core_left.astype(jnp.float32)
    projected_part = jnp.dot(left_float, range_part, precision=highest)
    every = ("row", "col")
    projected = gather_rows(scatter_sum(projected_part, every, nrow * ncol), every, nrow * ncol)
    projected, range_part, own_columns = lax.optimization_barrier(
        (projected, range_part, own_columns)
    )
    own_columns = gather_rows(scatter_sum(own_columns, "row", nrow), "row", nrow)
    range_sketch = gather_rows(scatter_sum(range_part, "col", ncol), "col", ncol)
    gram_matrix = jnp.dot(projected.T, projected, precision=highest)
    right_hand = jnp.dot(projected.T, own_columns, precision=highest)
    core_solution = cholesky_solve(gram_matrix, right_hand)
    return (range_sketch, corange_sketch, core_solution)


def solution(mesh):
    in_specs = (
        P(("row", "col"), None),
        P("row", "col"),
        P("col", None),
        P(None, "row"),
        P(None, "row"),
        P(None, "col"),
    )
    out_specs = (P("row", None), P(None, "col"), P(None, "col"))
    return jax.shard_map(local, mesh=mesh, in_specs=in_specs, out_specs=out_specs, check_vma=False)
```

```python
import jax
import jax.numpy as jnp
from jax import lax
from jax.sharding import PartitionSpec as P

S = 768


def scatter_sum(part, axis, groups):
    rows = part.shape[0] // groups
    got = lax.all_to_all(part, axis, split_axis=0, concat_axis=0, tiled=True)
    return got.reshape(groups, rows, *part.shape[1:]).sum(axis=0)


def gather_rows(chunk, axis, groups):
    tiled = jnp.broadcast_to(chunk[None], (groups, *chunk.shape)).reshape(
        groups * chunk.shape[0], *chunk.shape[1:]
    )
    return lax.all_to_all(tiled, axis, split_axis=0, concat_axis=0, tiled=True)


def dot_hi(a, b):
    return jnp.dot(a, b, precision=lax.Precision.HIGHEST)


def cholesky_solve(gram, rhs, size=128):
    count = gram.shape[0] // size
    gram = (gram + gram.T) * 0.5
    block = lambda i, j: gram[i * size:(i + 1) * size, j * size:(j + 1) * size]
    eye = jnp.eye(size, dtype=gram.dtype)
    low = {}
    inverse = []
    for j in range(count):
        a = block(j, j)
        for m in range(j):
            a = a - dot_hi(low[j, m], low[j, m].T)
        low[j, j] = lax.linalg.cholesky(a, symmetrize_input=False)
        inverse.append(lax.linalg.triangular_solve(low[j, j], eye, left_side=True, lower=True))
        for i in range(j + 1, count):
            a = block(i, j)
            for m in range(j):
                a = a - dot_hi(low[i, m], low[j, m].T)
            low[i, j] = dot_hi(a, inverse[j].T)
    halfway = []
    for i in range(count):
        r = rhs[i * size:(i + 1) * size]
        for m in range(i):
            r = r - dot_hi(low[i, m], halfway[m])
        halfway.append(dot_hi(inverse[i], r))
    result = [None] * count
    for i in reversed(range(count)):
        r = halfway[i]
        for m in range(i + 1, count):
            r = r - dot_hi(low[m, i].T, result[m])
        result[i] = dot_hi(inverse[i].T, r)
    return jnp.concatenate(result, axis=0)


def local(adjusted_rows, base_weight, range_test, corange_test, core_left, core_right):
    highest = lax.Precision.HIGHEST
    ncol = lax.axis_size("col")
    nrow = lax.axis_size("row")
    height, width = adjusted_rows.shape[0], adjusted_rows.shape[1] // ncol
    by_target = adjusted_rows.reshape(height, ncol, width).transpose(1, 0, 2)
    adjusted_block = lax.all_to_all(by_target, "col", split_axis=0, concat_axis=0, tiled=True)
    adjusted_block = adjusted_block.reshape(ncol * height, width)
    difference = (adjusted_block.astype(jnp.float32) - base_weight.astype(jnp.float32)).astype(
        jnp.bfloat16
    )
    left_product = jnp.dot(core_left, difference, preferred_element_type=jnp.float32)
    partial_value = jnp.dot(left_product, core_right.astype(jnp.float32).T, precision=highest)
    own_columns = lax.psum_scatter(partial_value, "col", scatter_dimension=1, tiled=True)
    corange_part = jnp.dot(corange_test, difference, preferred_element_type=jnp.float32)
    corange_sketch = lax.psum(corange_part, "row")
    range_part = jnp.dot(difference, range_test, preferred_element_type=jnp.float32)
    left_float = core_left.astype(jnp.float32)
    projected_part = jnp.dot(left_float, range_part, precision=highest)
    every = ("row", "col")
    projected = gather_rows(scatter_sum(projected_part, every, nrow * ncol), every, nrow * ncol)
    projected, range_part, own_columns = lax.optimization_barrier(
        (projected, range_part, own_columns)
    )
    range_sketch = gather_rows(scatter_sum(range_part, "col", ncol), "col", ncol)
    range_sketch, own_columns = lax.optimization_barrier((range_sketch, own_columns))
    own_columns = gather_rows(scatter_sum(own_columns, "row", nrow), "row", nrow)
    gram_matrix = jnp.dot(projected.T, projected, precision=highest)
    right_hand = jnp.dot(projected.T, own_columns, precision=highest)
    core_solution = cholesky_solve(gram_matrix, right_hand)
    return (range_sketch, corange_sketch, core_solution)


def solution(mesh):
    in_specs = (
        P(("row", "col"), None),
        P("row", "col"),
        P("col", None),
        P(None, "row"),
        P(None, "row"),
        P(None, "col"),
    )
    out_specs = (P("row", None), P(None, "col"), P(None, "col"))
    return jax.shard_map(local, mesh=mesh, in_specs=in_specs, out_specs=out_specs, check_vma=False)
```

```python
import jax
import jax.numpy as jnp
from jax import lax
from jax.sharding import PartitionSpec as P

S = 768


def scatter_sum(part, axis, groups):
    rows = part.shape[0] // groups
    got = lax.all_to_all(part, axis, split_axis=0, concat_axis=0, tiled=True)
    return got.reshape(groups, rows, *part.shape[1:]).sum(axis=0)


def gather_rows(chunk, axis, groups):
    tiled = jnp.broadcast_to(chunk[None], (groups, *chunk.shape)).reshape(
        groups * chunk.shape[0], *chunk.shape[1:]
    )
    return lax.all_to_all(tiled, axis, split_axis=0, concat_axis=0, tiled=True)


def dot_hi(a, b):
    return jnp.dot(a, b, precision=lax.Precision.HIGHEST)


def cholesky_solve(gram, rhs, size=128):
    count = gram.shape[0] // size
    gram = (gram + gram.T) * 0.5
    block = lambda i, j: gram[i * size:(i + 1) * size, j * size:(j + 1) * size]
    eye = jnp.eye(size, dtype=gram.dtype)
    low = {}
    inverse = []
    for j in range(count):
        a = block(j, j)
        for m in range(j):
            a = a - dot_hi(low[j, m], low[j, m].T)
        low[j, j] = lax.linalg.cholesky(a, symmetrize_input=False)
        inverse.append(lax.linalg.triangular_solve(low[j, j], eye, left_side=True, lower=True))
        for i in range(j + 1, count):
            a = block(i, j)
            for m in range(j):
                a = a - dot_hi(low[i, m], low[j, m].T)
            low[i, j] = dot_hi(a, inverse[j].T)
    halfway = []
    for i in range(count):
        r = rhs[i * size:(i + 1) * size]
        for m in range(i):
            r = r - dot_hi(low[i, m], halfway[m])
        halfway.append(dot_hi(inverse[i], r))
    result = [None] * count
    for i in reversed(range(count)):
        r = halfway[i]
        for m in range(i + 1, count):
            r = r - dot_hi(low[m, i].T, result[m])
        result[i] = dot_hi(inverse[i].T, r)
    return jnp.concatenate(result, axis=0)


def local(adjusted_rows, base_weight, range_test, corange_test, core_left, core_right):
    highest = lax.Precision.HIGHEST
    ncol = lax.axis_size("col")
    nrow = lax.axis_size("row")
    height, width = adjusted_rows.shape[0], adjusted_rows.shape[1] // ncol
    by_target = adjusted_rows.reshape(height, ncol, width).transpose(1, 0, 2)
    adjusted_block = lax.all_to_all(by_target, "col", split_axis=0, concat_axis=0, tiled=True)
    adjusted_block = adjusted_block.reshape(ncol * height, width)
    difference = (adjusted_block.astype(jnp.float32) - base_weight.astype(jnp.float32)).astype(
        jnp.bfloat16
    )
    left_product = jnp.dot(core_left, difference, preferred_element_type=jnp.float32)
    partial_value = jnp.dot(left_product, core_right.astype(jnp.float32).T, precision=highest)
    own_columns = lax.psum_scatter(partial_value, "col", scatter_dimension=1, tiled=True)
    corange_part = jnp.dot(corange_test, difference, preferred_element_type=jnp.float32)
    corange_sketch = lax.psum(corange_part, "row")
    range_part = jnp.dot(difference, range_test, preferred_element_type=jnp.float32)
    left_float = core_left.astype(jnp.float32)
    projected_part = jnp.dot(left_float, range_part, precision=highest)
    projected = scatter_sum(scatter_sum(projected_part, "col", ncol), "row", nrow)
    projected = gather_rows(gather_rows(projected, "row", nrow), "col", ncol)
    projected, range_part, own_columns = lax.optimization_barrier(
        (projected, range_part, own_columns)
    )
    range_sketch = gather_rows(scatter_sum(range_part, "col", ncol), "col", ncol)
    range_sketch, own_columns = lax.optimization_barrier((range_sketch, own_columns))
    own_columns = gather_rows(scatter_sum(own_columns, "row", nrow), "row", nrow)
    gram_matrix = jnp.dot(projected.T, projected, precision=highest)
    right_hand = jnp.dot(projected.T, own_columns, precision=highest)
    core_solution = cholesky_solve(gram_matrix, right_hand)
    return (range_sketch, corange_sketch, core_solution)


def solution(mesh):
    in_specs = (
        P(("row", "col"), None),
        P("row", "col"),
        P("col", None),
        P(None, "row"),
        P(None, "row"),
        P(None, "col"),
    )
    out_specs = (P("row", None), P(None, "col"), P(None, "col"))
    return jax.shard_map(local, mesh=mesh, in_specs=in_specs, out_specs=out_specs, check_vma=False)
```

```python
import jax
import jax.numpy as jnp
from jax import lax
from jax.sharding import PartitionSpec as P

S = 768


def scatter_sum(part, axis, groups):
    rows = part.shape[0] // groups
    got = lax.all_to_all(part, axis, split_axis=0, concat_axis=0, tiled=True)
    return got.reshape(groups, rows, *part.shape[1:]).sum(axis=0)


def gather_rows(chunk, axis, groups):
    tiled = jnp.broadcast_to(chunk[None], (groups, *chunk.shape)).reshape(
        groups * chunk.shape[0], *chunk.shape[1:]
    )
    return lax.all_to_all(tiled, axis, split_axis=0, concat_axis=0, tiled=True)


def dot_hi(a, b):
    return jnp.dot(a, b, precision=lax.Precision.HIGHEST)


def cholesky_solve(gram, rhs, size=128):
    count = gram.shape[0] // size
    gram = (gram + gram.T) * 0.5
    block = lambda i, j: gram[i * size:(i + 1) * size, j * size:(j + 1) * size]
    eye = jnp.eye(size, dtype=gram.dtype)
    low = {}
    inverse = []
    for j in range(count):
        a = block(j, j)
        for m in range(j):
            a = a - dot_hi(low[j, m], low[j, m].T)
        low[j, j] = lax.linalg.cholesky(a, symmetrize_input=False)
        inverse.append(lax.linalg.triangular_solve(low[j, j], eye, left_side=True, lower=True))
        for i in range(j + 1, count):
            a = block(i, j)
            for m in range(j):
                a = a - dot_hi(low[i, m], low[j, m].T)
            low[i, j] = dot_hi(a, inverse[j].T)
    halfway = []
    for i in range(count):
        r = rhs[i * size:(i + 1) * size]
        for m in range(i):
            r = r - dot_hi(low[i, m], halfway[m])
        halfway.append(dot_hi(inverse[i], r))
    result = [None] * count
    for i in reversed(range(count)):
        r = halfway[i]
        for m in range(i + 1, count):
            r = r - dot_hi(low[m, i].T, result[m])
        result[i] = dot_hi(inverse[i].T, r)
    return jnp.concatenate(result, axis=0)


def local(adjusted_rows, base_weight, range_test, corange_test, core_left, core_right):
    highest = lax.Precision.HIGHEST
    ncol = lax.axis_size("col")
    nrow = lax.axis_size("row")
    height, width = adjusted_rows.shape[0], adjusted_rows.shape[1] // ncol
    by_target = adjusted_rows.reshape(height, ncol, width).transpose(1, 0, 2)
    adjusted_block = lax.all_to_all(by_target, "col", split_axis=0, concat_axis=0, tiled=True)
    adjusted_block = adjusted_block.reshape(ncol * height, width)
    difference = (adjusted_block.astype(jnp.float32) - base_weight.astype(jnp.float32)).astype(
        jnp.bfloat16
    )
    left_product = jnp.dot(core_left, difference, preferred_element_type=jnp.float32)
    partial_value = jnp.dot(left_product, core_right.astype(jnp.float32).T, precision=highest)
    own_columns = lax.psum_scatter(partial_value, "col", scatter_dimension=1, tiled=True)
    own_columns = lax.psum(own_columns, "row")
    corange_part = jnp.dot(corange_test, difference, preferred_element_type=jnp.float32)
    corange_sketch = lax.psum(corange_part, "row")
    range_part = jnp.dot(difference, range_test, preferred_element_type=jnp.float32)
    left_float = core_left.astype(jnp.float32)
    projected_part = jnp.dot(left_float, range_part, precision=highest)
    projected = scatter_sum(scatter_sum(projected_part, "col", ncol), "row", nrow)
    projected = gather_rows(gather_rows(projected, "row", nrow), "col", ncol)
    projected, range_part = lax.optimization_barrier((projected, range_part))
    range_sketch = gather_rows(scatter_sum(range_part, "col", ncol), "col", ncol)
    gram_matrix = jnp.dot(projected.T, projected, precision=highest)
    right_hand = jnp.dot(projected.T, own_columns, precision=highest)
    core_solution = cholesky_solve(gram_matrix, right_hand)
    return (range_sketch, corange_sketch, core_solution)


def solution(mesh):
    in_specs = (
        P(("row", "col"), None),
        P("row", "col"),
        P("col", None),
        P(None, "row"),
        P(None, "row"),
        P(None, "col"),
    )
    out_specs = (P("row", None), P(None, "col"), P(None, "col"))
    return jax.shard_map(local, mesh=mesh, in_specs=in_specs, out_specs=out_specs, check_vma=False)
```

```python
import jax
import jax.numpy as jnp
from jax import lax
from jax.sharding import PartitionSpec as P

S = 768


def scatter_sum(part, axis, groups):
    rows = part.shape[0] // groups
    got = lax.all_to_all(part, axis, split_axis=0, concat_axis=0, tiled=True)
    return got.reshape(groups, rows, *part.shape[1:]).sum(axis=0)


def gather_rows(chunk, axis, groups):
    tiled = jnp.broadcast_to(chunk[None], (groups, *chunk.shape)).reshape(
        groups * chunk.shape[0], *chunk.shape[1:]
    )
    return lax.all_to_all(tiled, axis, split_axis=0, concat_axis=0, tiled=True)


def dot_hi(a, b):
    return jnp.dot(a, b, precision=lax.Precision.HIGHEST)


def cholesky_solve(gram, rhs, size=128):
    count = gram.shape[0] // size
    gram = (gram + gram.T) * 0.5
    block = lambda i, j: gram[i * size:(i + 1) * size, j * size:(j + 1) * size]
    eye = jnp.eye(size, dtype=gram.dtype)
    low = {}
    inverse = []
    for j in range(count):
        a = block(j, j)
        for m in range(j):
            a = a - dot_hi(low[j, m], low[j, m].T)
        low[j, j] = lax.linalg.cholesky(a, symmetrize_input=False)
        inverse.append(lax.linalg.triangular_solve(low[j, j], eye, left_side=True, lower=True))
        for i in range(j + 1, count):
            a = block(i, j)
            for m in range(j):
                a = a - dot_hi(low[i, m], low[j, m].T)
            low[i, j] = dot_hi(a, inverse[j].T)
    halfway = []
    for i in range(count):
        r = rhs[i * size:(i + 1) * size]
        for m in range(i):
            r = r - dot_hi(low[i, m], halfway[m])
        halfway.append(dot_hi(inverse[i], r))
    result = [None] * count
    for i in reversed(range(count)):
        r = halfway[i]
        for m in range(i + 1, count):
            r = r - dot_hi(low[m, i].T, result[m])
        result[i] = dot_hi(inverse[i].T, r)
    return jnp.concatenate(result, axis=0)


def local(adjusted_rows, base_weight, range_test, corange_test, core_left, core_right):
    highest = lax.Precision.HIGHEST
    ncol = lax.axis_size("col")
    nrow = lax.axis_size("row")
    height, width = adjusted_rows.shape[0], adjusted_rows.shape[1] // ncol
    by_target = adjusted_rows.reshape(height, ncol, width).transpose(1, 0, 2)
    adjusted_block = lax.all_to_all(by_target, "col", split_axis=0, concat_axis=0, tiled=True)
    adjusted_block = adjusted_block.reshape(ncol * height, width)
    difference = (adjusted_block.astype(jnp.float32) - base_weight.astype(jnp.float32)).astype(
        jnp.bfloat16
    )
    left_product = jnp.dot(core_left, difference, preferred_element_type=jnp.float32)
    partial_value = jnp.dot(left_product, core_right.astype(jnp.float32).T, precision=highest)
    own_columns = lax.psum_scatter(partial_value, "col", scatter_dimension=1, tiled=True)
    own_columns = lax.psum_scatter(own_columns, "row", scatter_dimension=0, tiled=True)
    own_columns = lax.all_gather(own_columns, "row", axis=0, tiled=True)
    corange_part = jnp.dot(corange_test, difference, preferred_element_type=jnp.float32)
    corange_sketch = lax.psum(corange_part, "row")
    range_part = jnp.dot(difference, range_test, preferred_element_type=jnp.float32)
    left_float = core_left.astype(jnp.float32)
    projected_part = jnp.dot(left_float, range_part, precision=highest)
    projected = scatter_sum(scatter_sum(projected_part, "col", ncol), "row", nrow)
    projected = gather_rows(gather_rows(projected, "row", nrow), "col", ncol)
    projected, range_part = lax.optimization_barrier((projected, range_part))
    range_sketch = gather_rows(scatter_sum(range_part, "col", ncol), "col", ncol)
    gram_matrix = jnp.dot(projected.T, projected, precision=highest)
    right_hand = jnp.dot(projected.T, own_columns, precision=highest)
    core_solution = cholesky_solve(gram_matrix, right_hand)
    return (range_sketch, corange_sketch, core_solution)


def solution(mesh):
    in_specs = (
        P(("row", "col"), None),
        P("row", "col"),
        P("col", None),
        P(None, "row"),
        P(None, "row"),
        P(None, "col"),
    )
    out_specs = (P("row", None), P(None, "col"), P(None, "col"))
    return jax.shard_map(local, mesh=mesh, in_specs=in_specs, out_specs=out_specs, check_vma=False)
```

```python
import jax
import jax.numpy as jnp
from jax import lax
from jax.sharding import PartitionSpec as P
from jax.experimental import pallas as pl
from jax.experimental.pallas import tpu as pltpu

S = 768


def scatter_sum(part, axis, groups):
    rows = part.shape[0] // groups
    got = lax.all_to_all(part, axis, split_axis=0, concat_axis=0, tiled=True)
    return got.reshape(groups, rows, *part.shape[1:]).sum(axis=0)


def gather_rows(chunk, axis, groups):
    tiled = jnp.broadcast_to(chunk[None], (groups, *chunk.shape)).reshape(
        groups * chunk.shape[0], *chunk.shape[1:]
    )
    return lax.all_to_all(tiled, axis, split_axis=0, concat_axis=0, tiled=True)


def split_columns(rows, parts):
    height, width = rows.shape[0], rows.shape[1] // parts

    def kernel(x_ref, o_ref):
        for j in range(parts):
            o_ref[j] = x_ref[:, j * width:(j + 1) * width]

    return pl.pallas_call(
        kernel,
        out_shape=jax.ShapeDtypeStruct((parts, height, width), rows.dtype),
        compiler_params=pltpu.CompilerParams(vmem_limit_bytes=48 * 1024 * 1024),
    )(rows)


def dot_hi(a, b):
    return jnp.dot(a, b, precision=lax.Precision.HIGHEST)


def cholesky_solve(gram, rhs, size=128):
    count = gram.shape[0] // size
    gram = (gram + gram.T) * 0.5
    block = lambda i, j: gram[i * size:(i + 1) * size, j * size:(j + 1) * size]
    eye = jnp.eye(size, dtype=gram.dtype)
    low = {}
    inverse = []
    for j in range(count):
        a = block(j, j)
        for m in range(j):
            a = a - dot_hi(low[j, m], low[j, m].T)
        low[j, j] = lax.linalg.cholesky(a, symmetrize_input=False)
        inverse.append(lax.linalg.triangular_solve(low[j, j], eye, left_side=True, lower=True))
        for i in range(j + 1, count):
            a = block(i, j)
            for m in range(j):
                a = a - dot_hi(low[i, m], low[j, m].T)
            low[i, j] = dot_hi(a, inverse[j].T)
    halfway = []
    for i in range(count):
        r = rhs[i * size:(i + 1) * size]
        for m in range(i):
            r = r - dot_hi(low[i, m], halfway[m])
        halfway.append(dot_hi(inverse[i], r))
    result = [None] * count
    for i in reversed(range(count)):
        r = halfway[i]
        for m in range(i + 1, count):
            r = r - dot_hi(low[m, i].T, result[m])
        result[i] = dot_hi(inverse[i].T, r)
    return jnp.concatenate(result, axis=0)


def local(adjusted_rows, base_weight, range_test, corange_test, core_left, core_right):
    highest = lax.Precision.HIGHEST
    ncol = lax.axis_size("col")
    nrow = lax.axis_size("row")
    height, width = adjusted_rows.shape[0], adjusted_rows.shape[1] // ncol
    by_target = split_columns(adjusted_rows, ncol)
    adjusted_block = lax.all_to_all(by_target, "col", split_axis=0, concat_axis=0, tiled=True)
    adjusted_block = adjusted_block.reshape(ncol * height, width)
    difference = (adjusted_block.astype(jnp.float32) - base_weight.astype(jnp.float32)).astype(
        jnp.bfloat16
    )
    left_product = jnp.dot(core_left, difference, preferred_element_type=jnp.float32)
    partial_value = jnp.dot(left_product, core_right.astype(jnp.float32).T, precision=highest)
    own_columns = lax.psum_scatter(partial_value, "col", scatter_dimension=1, tiled=True)
    own_columns = lax.psum(own_columns, "row")
    corange_part = jnp.dot(corange_test, difference, preferred_element_type=jnp.float32)
    corange_sketch = lax.psum(corange_part, "row")
    range_part = jnp.dot(difference, range_test, preferred_element_type=jnp.float32)
    left_float = core_left.astype(jnp.float32)
    projected_part = jnp.dot(left_float, range_part, precision=highest)
    projected = scatter_sum(scatter_sum(projected_part, "col", ncol), "row", nrow)
    projected = gather_rows(gather_rows(projected, "row", nrow), "col", ncol)
    projected, range_part = lax.optimization_barrier((projected, range_part))
    range_sketch = gather_rows(scatter_sum(range_part, "col", ncol), "col", ncol)
    gram_matrix = jnp.dot(projected.T, projected, precision=highest)
    right_hand = jnp.dot(projected.T, own_columns, precision=highest)
    core_solution = cholesky_solve(gram_matrix, right_hand)
    return (range_sketch, corange_sketch, core_solution)


def solution(mesh):
    in_specs = (
        P(("row", "col"), None),
        P("row", "col"),
        P("col", None),
        P(None, "row"),
        P(None, "row"),
        P(None, "col"),
    )
    out_specs = (P("row", None), P(None, "col"), P(None, "col"))
    return jax.shard_map(local, mesh=mesh, in_specs=in_specs, out_specs=out_specs, check_vma=False)
```

```python
import jax
import jax.numpy as jnp
from jax import lax
from jax.sharding import PartitionSpec as P

S = 768


def scatter_sum(part, axis, groups):
    rows = part.shape[0] // groups
    got = lax.all_to_all(part, axis, split_axis=0, concat_axis=0, tiled=True)
    return got.reshape(groups, rows, *part.shape[1:]).sum(axis=0)


def gather_rows(chunk, axis, groups):
    tiled = jnp.broadcast_to(chunk[None], (groups, *chunk.shape)).reshape(
        groups * chunk.shape[0], *chunk.shape[1:]
    )
    return lax.all_to_all(tiled, axis, split_axis=0, concat_axis=0, tiled=True)


def dot_hi(a, b):
    return jnp.dot(a, b, precision=lax.Precision.HIGHEST)


def cholesky_solve(gram, rhs, size=128):
    count = gram.shape[0] // size
    gram = (gram + gram.T) * 0.5
    block = lambda i, j: gram[i * size:(i + 1) * size, j * size:(j + 1) * size]
    eye = jnp.eye(size, dtype=gram.dtype)
    low = {}
    inverse = []
    for j in range(count):
        a = block(j, j)
        for m in range(j):
            a = a - dot_hi(low[j, m], low[j, m].T)
        low[j, j] = lax.linalg.cholesky(a, symmetrize_input=False)
        inverse.append(lax.linalg.triangular_solve(low[j, j], eye, left_side=True, lower=True))
        for i in range(j + 1, count):
            a = block(i, j)
            for m in range(j):
                a = a - dot_hi(low[i, m], low[j, m].T)
            low[i, j] = dot_hi(a, inverse[j].T)
    halfway = []
    for i in range(count):
        r = rhs[i * size:(i + 1) * size]
        for m in range(i):
            r = r - dot_hi(low[i, m], halfway[m])
        halfway.append(dot_hi(inverse[i], r))
    result = [None] * count
    for i in reversed(range(count)):
        r = halfway[i]
        for m in range(i + 1, count):
            r = r - dot_hi(low[m, i].T, result[m])
        result[i] = dot_hi(inverse[i].T, r)
    return jnp.concatenate(result, axis=0)


def local(adjusted_rows, base_weight, range_test, corange_test, core_left, core_right):
    highest = lax.Precision.HIGHEST
    ncol = lax.axis_size("col")
    nrow = lax.axis_size("row")
    height, width = adjusted_rows.shape[0], adjusted_rows.shape[1] // ncol
    by_target = adjusted_rows.reshape(height, ncol, width).transpose(1, 0, 2)
    adjusted_block = lax.all_to_all(by_target, "col", split_axis=0, concat_axis=0, tiled=True)
    adjusted_block = adjusted_block.reshape(ncol * height, width)
    difference = (adjusted_block.astype(jnp.float32) - base_weight.astype(jnp.float32)).astype(
        jnp.bfloat16
    )
    corange_part = jnp.dot(corange_test, difference, preferred_element_type=jnp.float32)
    corange_sketch = lax.psum(corange_part, "row")
    left_product = jnp.dot(core_left, difference, preferred_element_type=jnp.float32)
    partial_value = jnp.dot(left_product, core_right.astype(jnp.float32).T, precision=highest)
    own_columns = lax.psum_scatter(partial_value, "col", scatter_dimension=1, tiled=True)
    own_columns, corange_sketch = lax.optimization_barrier((own_columns, corange_sketch))
    own_columns = lax.psum(own_columns, "row")
    range_part = jnp.dot(difference, range_test, preferred_element_type=jnp.float32)
    left_float = core_left.astype(jnp.float32)
    projected_part = jnp.dot(left_float, range_part, precision=highest)
    projected = scatter_sum(scatter_sum(projected_part, "col", ncol), "row", nrow)
    projected = gather_rows(gather_rows(projected, "row", nrow), "col", ncol)
    projected, range_part = lax.optimization_barrier((projected, range_part))
    range_sketch = gather_rows(scatter_sum(range_part, "col", ncol), "col", ncol)
    gram_matrix = jnp.dot(projected.T, projected, precision=highest)
    right_hand = jnp.dot(projected.T, own_columns, precision=highest)
    core_solution = cholesky_solve(gram_matrix, right_hand)
    return (range_sketch, corange_sketch, core_solution)


def solution(mesh):
    in_specs = (
        P(("row", "col"), None),
        P("row", "col"),
        P("col", None),
        P(None, "row"),
        P(None, "row"),
        P(None, "col"),
    )
    out_specs = (P("row", None), P(None, "col"), P(None, "col"))
    return jax.shard_map(local, mesh=mesh, in_specs=in_specs, out_specs=out_specs, check_vma=False)
```

```python
import jax
import jax.numpy as jnp
from jax import lax
from jax.sharding import PartitionSpec as P

S = 768


def scatter_sum(part, axis, groups):
    rows = part.shape[0] // groups
    got = lax.all_to_all(part, axis, split_axis=0, concat_axis=0, tiled=True)
    return got.reshape(groups, rows, *part.shape[1:]).sum(axis=0)


def gather_rows(chunk, axis, groups):
    tiled = jnp.broadcast_to(chunk[None], (groups, *chunk.shape)).reshape(
        groups * chunk.shape[0], *chunk.shape[1:]
    )
    return lax.all_to_all(tiled, axis, split_axis=0, concat_axis=0, tiled=True)


def dot_exact(wide, narrow):
    high = wide.astype(jnp.bfloat16)
    rest = wide - high.astype(jnp.float32)
    middle = rest.astype(jnp.bfloat16)
    low = (rest - middle.astype(jnp.float32)).astype(jnp.bfloat16)
    out = [jnp.dot(piece, narrow, preferred_element_type=jnp.float32) for piece in (high, middle, low)]
    return out[0] + (out[1] + out[2])


def dot_hi(a, b):
    return jnp.dot(a, b, precision=lax.Precision.HIGHEST)


def cholesky_solve(gram, rhs, size=128):
    count = gram.shape[0] // size
    gram = (gram + gram.T) * 0.5
    block = lambda i, j: gram[i * size:(i + 1) * size, j * size:(j + 1) * size]
    eye = jnp.eye(size, dtype=gram.dtype)
    low = {}
    inverse = []
    for j in range(count):
        a = block(j, j)
        for m in range(j):
            a = a - dot_hi(low[j, m], low[j, m].T)
        low[j, j] = lax.linalg.cholesky(a, symmetrize_input=False)
        inverse.append(lax.linalg.triangular_solve(low[j, j], eye, left_side=True, lower=True))
        for i in range(j + 1, count):
            a = block(i, j)
            for m in range(j):
                a = a - dot_hi(low[i, m], low[j, m].T)
            low[i, j] = dot_hi(a, inverse[j].T)
    halfway = []
    for i in range(count):
        r = rhs[i * size:(i + 1) * size]
        for m in range(i):
            r = r - dot_hi(low[i, m], halfway[m])
        halfway.append(dot_hi(inverse[i], r))
    result = [None] * count
    for i in reversed(range(count)):
        r = halfway[i]
        for m in range(i + 1, count):
            r = r - dot_hi(low[m, i].T, result[m])
        result[i] = dot_hi(inverse[i].T, r)
    return jnp.concatenate(result, axis=0)


def local(adjusted_rows, base_weight, range_test, corange_test, core_left, core_right):
    highest = lax.Precision.HIGHEST
    ncol = lax.axis_size("col")
    nrow = lax.axis_size("row")
    height, width = adjusted_rows.shape[0], adjusted_rows.shape[1] // ncol
    by_target = adjusted_rows.reshape(height, ncol, width).transpose(1, 0, 2)
    adjusted_block = lax.all_to_all(by_target, "col", split_axis=0, concat_axis=0, tiled=True)
    adjusted_block = adjusted_block.reshape(ncol * height, width)
    difference = (adjusted_block.astype(jnp.float32) - base_weight.astype(jnp.float32)).astype(
        jnp.bfloat16
    )
    left_product = jnp.dot(core_left, difference, preferred_element_type=jnp.float32)
    partial_value = dot_exact(left_product, core_right.T)
    own_columns = lax.psum_scatter(partial_value, "col", scatter_dimension=1, tiled=True)
    own_columns = lax.psum(own_columns, "row")
    corange_part = jnp.dot(corange_test, difference, preferred_element_type=jnp.float32)
    corange_sketch = lax.psum(corange_part, "row")
    range_part = jnp.dot(difference, range_test, preferred_element_type=jnp.float32)
    left_float = core_left.astype(jnp.float32)
    projected_part = jnp.dot(left_float, range_part, precision=highest)
    projected = scatter_sum(scatter_sum(projected_part, "col", ncol), "row", nrow)
    projected = gather_rows(gather_rows(projected, "row", nrow), "col", ncol)
    projected, range_part = lax.optimization_barrier((projected, range_part))
    range_sketch = gather_rows(scatter_sum(range_part, "col", ncol), "col", ncol)
    gram_matrix = jnp.dot(projected.T, projected, precision=highest)
    right_hand = jnp.dot(projected.T, own_columns, precision=highest)
    core_solution = cholesky_solve(gram_matrix, right_hand)
    return (range_sketch, corange_sketch, core_solution)


def solution(mesh):
    in_specs = (
        P(("row", "col"), None),
        P("row", "col"),
        P("col", None),
        P(None, "row"),
        P(None, "row"),
        P(None, "col"),
    )
    out_specs = (P("row", None), P(None, "col"), P(None, "col"))
    return jax.shard_map(local, mesh=mesh, in_specs=in_specs, out_specs=out_specs, check_vma=False)
```
